512 devices in a mesh: resp: 64 (over y_lo, z, core), mp: 8 (over y_hi, x).
Axes of the slice: x: 4, y: 8 (y_hi: 2, y_lo: 4; y = y_hi * 4 + y_lo), z: 8, core: 2. Of those that a mesh axis runs over, the one named last changes fastest.
Arguments:
- queries: bfloat16 [16384, 64, 128], P('resp', 'mp'), may hold values from -200 to 200
- response_kv: bfloat16 [16384, 2, 8, 128], P('resp', None, 'mp'), may hold values from -6 to 6
- prefix_kv: bfloat16 [4096, 2, 8, 128], P(('resp', 'mp')), may hold values from -8 to 8
- lengths: int32 [64], P('resp'), may hold values from 128 to 256, as said below
- score_weight: float32 [8192], P('mp'), may hold values from -30 to 30
Outputs:
- attended: bfloat16 [16384, 8192], P('resp', 'mp')
- score: float32 [64], P('resp')
The draws below stay inside these ranges and needn't reach their ends.
Inputs may be any that keep to these rules, and one draw needn't show every extreme that they name: `lengths`: every length is a multiple of 128; some response is full and some has one tile.
All inputs are finite; a program needn't handle non-finite values.
Results may differ from the reference program's by a relative error of at most 0.0045.
Values may be sent and summed in bfloat16 or wider, within the bound.
No kernel may reach another device: no remote copies, remote signals or barrier semaphores. Data moves between devices by JAX's collectives and lax.ppermute only.
A program may use at most 64 MiB of HBM per device.

```python
import math
import jax
import jax.numpy as jnp
from jax import lax

H = 64
KVH = 8
HD = 128
RESP = 256
TILE = 128
RESPONSES = 64
PREFIX = 4096


def prefix_cache(key):
    raw = jnp.clip(jax.random.normal(jax.random.fold_in(key, 11), (PREFIX, 2, KVH, HD), jnp.float32), -6.0, 6.0)
    return raw


def draw_prefix_kv(key, part):
    return prefix_cache(key).astype(jnp.bfloat16)


def draw_queries(key, part):
    base = 2.5 * jnp.clip(jax.random.normal(jax.random.fold_in(key, 23), (RESPONSES * RESP, H, HD), jnp.float32), -6.0, 6.0)
    return base.astype(jnp.bfloat16)


def draw_lengths(key, part):
    tiles = jax.random.randint(jax.random.fold_in(key, 37), (RESPONSES,), 1, RESP // TILE + 1)
    tiles = tiles.at[0].set(RESP // TILE)
    tiles = tiles.at[RESPONSES - 1].set(1)
    return (tiles * TILE).astype(jnp.int32)


def draw_score_weight(key, part):
    raw = jnp.clip(jax.random.normal(jax.random.fold_in(key, 41), (H * HD,), jnp.float32), -6.0, 6.0)
    heads = (jnp.arange(H * HD) // HD).astype(jnp.float32)
    rise = 3.0 ** (heads / (H - 1))
    return 0.5 * raw * rise


def steps_of(own_key, dims, shards, smallest, high):
    factor_of, own = 1.0, jax.random.fold_in(own_key, 6)
    for dim, parts in shards:
        steps = jnp.exp(jax.random.uniform(jax.random.fold_in(own, dim), (parts,), jnp.float32, smallest / len(shards), high / len(shards)))
        factor_of = factor_of * jnp.repeat(steps, dims[dim] // parts).reshape([-1 if axis == dim else 1 for axis in range(len(dims))])
    return factor_of


def noise(key, shape, spread, bound, cuts=(), held_as=jnp.bfloat16):
    entries = spread * jax.random.normal(key, shape, jnp.float32)
    if cuts:
        entries = entries * steps_of(key, shape, cuts, -0.22, 0.18)
    return jnp.clip(entries, -bound, bound).astype(held_as)


def setup_inputs(seed: int = 0) -> dict:
    arg_keys = jax.random.split(jax.random.key(seed), 6)
    queries = draw_queries(jax.random.fold_in(arg_keys[5], 71), 0)
    response_kv = noise(arg_keys[1], (RESPONSES * RESP, 2, KVH, HD), 1.0, 6.0, ((0, 64), (2, 8)))
    prefix_kv = draw_prefix_kv(jax.random.fold_in(arg_keys[5], 71), 0)
    lengths = draw_lengths(jax.random.fold_in(arg_keys[5], 71), 0)
    score_weight = draw_score_weight(jax.random.fold_in(arg_keys[5], 71), 0)
    return {"queries": queries, "response_kv": response_kv, "prefix_kv": prefix_kv, "lengths": lengths, "score_weight": score_weight}


def reference(queries, response_kv, prefix_kv, lengths, score_weight):
    group = H // KVH
    factor = 1.0 / math.sqrt(HD)
    cache = jnp.transpose(prefix_kv.astype(jnp.float32), (2, 1, 0, 3))
    asked = jnp.transpose(queries.astype(jnp.float32).reshape(RESPONSES, RESP, KVH, group, HD), (0, 2, 3, 1, 4))
    own = jnp.transpose(response_kv.astype(jnp.float32).reshape(RESPONSES, RESP, 2, KVH, HD), (0, 3, 2, 1, 4))
    positions = jnp.arange(RESP, dtype=jnp.int32)

    def per_response(item):
        asked_one, own_one, length = item
        allowed = (positions[None, :] <= positions[:, None]) & (positions[None, :] < length)

        def per_head(inner):
            query_block, mine, shared = inner
            far = jnp.einsum('qtd,sd->qts', query_block, shared[0]) * factor
            near = jnp.einsum('qtd,sd->qts', query_block, mine[0]) * factor
            near = jnp.where(allowed[None], near, jnp.float32(-1e+30))
            top = jnp.maximum(lax.optimization_barrier(jnp.max(far, axis=-1, keepdims=True)), lax.optimization_barrier(jnp.max(near, axis=-1, keepdims=True)))
            far_w = jnp.exp(far - top)
            near_w = jnp.where(allowed[None], jnp.exp(near - top), jnp.float32(0.0))
            total = lax.optimization_barrier(jnp.sum(far_w, axis=-1, keepdims=True)) + lax.optimization_barrier(jnp.sum(near_w, axis=-1, keepdims=True))
            far_b = lax.optimization_barrier(far_w.astype(jnp.bfloat16)).astype(jnp.float32)
            near_b = lax.optimization_barrier(near_w.astype(jnp.bfloat16)).astype(jnp.float32)
            mixed = jnp.einsum('qts,sd->qtd', far_b, shared[1]) + jnp.einsum('qts,sd->qtd', near_b, mine[1])
            return mixed / total
        heads = lax.map(per_head, (asked_one, own_one, cache))
        result = jnp.transpose(heads, (2, 0, 1, 3)).reshape(RESP, H * HD)
        result = jnp.where(positions[:, None] < length, result, jnp.float32(0.0))
        return result.astype(jnp.bfloat16)
    outs = lax.map(per_response, (asked, own, lengths))
    sums = lax.optimization_barrier(jnp.sum(outs.astype(jnp.float32) * score_weight[None, None, :], axis=(1, 2)))
    score = sums / lengths.astype(jnp.float32)
    return (outs.reshape(RESPONSES * RESP, H * HD), score)
```

```python
import math

import jax
import jax.numpy as jnp
import numpy as np
from jax import lax
from jax.sharding import PartitionSpec as P

neg_large = -1e30

resp_parts = (("y_lo", 4), ("z", 8), ("core", 2))
mp_parts = (("y_hi", 2), ("x", 4))
resp_axes = tuple(name for name, _ in resp_parts)
mp_axes = tuple(name for name, _ in mp_parts)
axis_size = dict(resp_parts + mp_parts)


def gather_by_all_to_all(x, axes):
    count = int(np.prod([axis_size[a] for a in axes]))
    copies = jnp.broadcast_to(x[None], (count,) + x.shape)
    got = lax.all_to_all(copies, axes, 0, 0, tiled=True)
    return got.reshape((count * x.shape[0],) + x.shape[1:])


def absorb(carry, keys, values, grouped, factor):
    best, total, accum = carry
    scores = jnp.einsum("grd,sgd->grs", grouped, keys, preferred_element_type=jnp.float32) * factor
    fresh = jnp.maximum(best, jnp.max(scores, axis=-1, keepdims=True))
    shrink = jnp.exp(best - fresh)
    weights = jnp.exp(scores - fresh)
    total = total * shrink + jnp.sum(weights, axis=-1, keepdims=True)
    accum = accum * shrink + jnp.einsum(
        "grs,sgd->grd", weights.astype(jnp.bfloat16), values, preferred_element_type=jnp.float32
    )
    return (fresh, total, accum)


def sweep(carry, whole_cache, grouped, factor):
    count = whole_cache.shape[0]
    block_len = math.gcd(count, 512)
    blocks = whole_cache.reshape((count // block_len, block_len) + whole_cache.shape[1:])

    def one_block(state, block):
        return (absorb(state, block[:, 0], block[:, 1], grouped, factor), None)

    carry, unused = lax.scan(one_block, carry, blocks)
    return carry


def per_device(queries, response_kv, prefix_kv, lengths, score_weight):
    resp_len = queries.shape[0]
    local_heads = queries.shape[1]
    head_size = queries.shape[2]
    local_kv = response_kv.shape[2]
    group = local_heads // local_kv
    rows = group * resp_len
    factor = 1.0 / math.sqrt(head_size)
    length = lengths[0]
    grouped = jnp.transpose(
        queries.reshape(resp_len, local_kv, group, head_size), (1, 2, 0, 3)
    ).reshape(local_kv, rows, head_size)
    key_pos = jnp.arange(resp_len, dtype=jnp.int32)[None, :]
    query_pos = (jnp.arange(rows, dtype=jnp.int32) % resp_len)[:, None]
    allowed = ((key_pos <= query_pos) & (key_pos < length))[None]
    near = (
        jnp.einsum("grd,sgd->grs", grouped, response_kv[:, 0], preferred_element_type=jnp.float32)
        * factor
    )
    near = jnp.where(allowed, near, neg_large)
    best = jnp.max(near, axis=-1, keepdims=True)
    near_w = jnp.where(allowed, jnp.exp(near - best), 0.0)
    total = jnp.sum(near_w, axis=-1, keepdims=True)
    accum = jnp.einsum(
        "grs,sgd->grd",
        near_w.astype(jnp.bfloat16),
        response_kv[:, 1],
        preferred_element_type=jnp.float32,
    )
    start_state = (best, total, accum)
    mine = lax.all_to_all(prefix_kv, mp_axes, split_axis=2, concat_axis=0, tiled=True)
    collected = gather_by_all_to_all(gather_by_all_to_all(mine, ("y_lo", "z")), ("core",))
    best, total, accum = sweep(start_state, collected, grouped, factor)
    mixed = (accum / total).reshape(local_kv, group, resp_len, head_size)
    mixed = jnp.transpose(mixed, (2, 0, 1, 3)).reshape(resp_len, local_heads * head_size)
    live = jnp.arange(resp_len, dtype=jnp.int32)[:, None] < length
    attended = jnp.where(live, mixed, 0.0).astype(jnp.bfloat16)
    partial_score = jnp.sum(attended.astype(jnp.float32) * score_weight[None, :])
    spread = jnp.broadcast_to(partial_score, (axis_size["y_hi"] * axis_size["x"],))
    summed = jnp.sum(lax.all_to_all(spread, mp_axes, 0, 0, tiled=True))
    score = (summed / length.astype(jnp.float32)).reshape(1)
    return (attended, score)


def solution(mesh):
    sizes = tuple(n for _, n in resp_parts) + tuple(n for _, n in mp_parts)
    fine = jax.sharding.Mesh(np.asarray(mesh.devices).reshape(sizes), resp_axes + mp_axes)
    R, M = resp_axes, mp_axes
    in_specs = (
        P(R, M, None),
        P(R, None, M, None),
        P(R + M, None, None, None),
        P(R),
        P(M),
    )
    out_specs = (P(R, M), P(R))
    return jax.shard_map(
        per_device, mesh=fine, in_specs=in_specs, out_specs=out_specs, check_vma=False
    )
```

```python
import functools
import math

import jax
import jax.numpy as jnp
import numpy as np
from jax import lax
from jax.experimental import pallas as pl
from jax.experimental.pallas import tpu as pltpu
from jax.sharding import PartitionSpec as P

neg_large = -1e30

resp_parts = (("y_lo", 4), ("z", 8), ("core", 2))
mp_parts = (("y_hi", 2), ("x", 4))
resp_axes = tuple(name for name, _ in resp_parts)
mp_axes = tuple(name for name, _ in mp_parts)
axis_size = dict(resp_parts + mp_parts)


def gather_by_all_to_all(x, axes):
    count = int(np.prod([axis_size[a] for a in axes]))
    copies = jnp.broadcast_to(x[None], (count,) + x.shape)
    got = lax.all_to_all(copies, axes, 0, 0, tiled=True)
    return got.reshape((count * x.shape[0],) + x.shape[1:])


def attend_kernel(length_ref, q_ref, far_ref, near_ref, out_ref, *, factor):
    length = length_ref[0]
    tokens, head_size = q_ref.shape
    q = q_ref[...]
    contract = (((1,), (1,)), ((), ()))
    far = lax.dot_general(q, far_ref[:, :head_size], contract, preferred_element_type=jnp.float32) * factor
    near = lax.dot_general(q, near_ref[:, :head_size], contract, preferred_element_type=jnp.float32) * factor
    query_pos = lax.broadcasted_iota(jnp.int32, near.shape, 0)
    key_pos = lax.broadcasted_iota(jnp.int32, near.shape, 1)
    allowed = (key_pos <= query_pos) & (key_pos < length)
    near = jnp.where(allowed, near, neg_large)
    top = jnp.maximum(jnp.max(far, axis=1, keepdims=True), jnp.max(near, axis=1, keepdims=True))
    far_w = jnp.exp(far - top)
    near_w = jnp.where(allowed, jnp.exp(near - top), 0.0)
    total = jnp.sum(far_w, axis=1, keepdims=True) + jnp.sum(near_w, axis=1, keepdims=True)
    mixed = jnp.dot(far_w.astype(jnp.bfloat16), far_ref[:, head_size:], preferred_element_type=jnp.float32)
    mixed = mixed + jnp.dot(near_w.astype(jnp.bfloat16), near_ref[:, head_size:], preferred_element_type=jnp.float32)
    mixed = mixed / total
    live = lax.broadcasted_iota(jnp.int32, mixed.shape, 0) < length
    out_ref[...] = jnp.where(live, mixed, 0.0).astype(out_ref.dtype)


def attend(lengths, queries, far_kv, near_kv):
    tokens, heads, head_size = queries.shape
    flat = queries.reshape(tokens, heads * head_size)
    keys = far_kv.shape[0]
    kernel = functools.partial(attend_kernel, factor=1.0 / math.sqrt(head_size))
    return pl.pallas_call(
        kernel,
        grid=(heads,),
        in_specs=[
            pl.BlockSpec(memory_space=pltpu.SMEM),
            pl.BlockSpec((tokens, head_size), lambda h: (0, h)),
            pl.BlockSpec((keys, 2 * head_size), lambda h: (0, 0)),
            pl.BlockSpec((tokens, 2 * head_size), lambda h: (0, 0)),
        ],
        out_specs=pl.BlockSpec((tokens, head_size), lambda h: (0, h)),
        out_shape=jax.ShapeDtypeStruct((tokens, heads * head_size), jnp.bfloat16),
    )(lengths, flat, far_kv, near_kv)


def per_device(queries, response_kv, prefix_kv, lengths, score_weight):
    resp_len, local_heads, head_size = queries.shape
    length = lengths[0]
    mine = lax.all_to_all(prefix_kv, mp_axes, split_axis=2, concat_axis=0, tiled=True)
    collected = gather_by_all_to_all(gather_by_all_to_all(mine, ("y_lo", "z")), ("core",))
    far_kv = collected.reshape(collected.shape[0], 2 * head_size)
    near_kv = response_kv.reshape(resp_len, 2 * head_size)
    attended = attend(lengths, queries, far_kv, near_kv)
    partial_score = jnp.sum(attended.astype(jnp.float32) * score_weight[None, :])
    spread = jnp.broadcast_to(partial_score, (axis_size["y_hi"] * axis_size["x"],))
    summed = jnp.sum(lax.all_to_all(spread, mp_axes, 0, 0, tiled=True))
    score = (summed / length.astype(jnp.float32)).reshape(1)
    return (attended, score)


def solution(mesh):
    sizes = tuple(n for _, n in resp_parts) + tuple(n for _, n in mp_parts)
    fine = jax.sharding.Mesh(np.asarray(mesh.devices).reshape(sizes), resp_axes + mp_axes)
    R, M = resp_axes, mp_axes
    in_specs = (
        P(R, M, None),
        P(R, None, M, None),
        P(R + M, None, None, None),
        P(R),
        P(M),
    )
    out_specs = (P(R, M), P(R))
    return jax.shard_map(
        per_device, mesh=fine, in_specs=in_specs, out_specs=out_specs, check_vma=False
    )
```

```python
import functools
import math

import jax
import jax.numpy as jnp
import numpy as np
from jax import lax
from jax.experimental import pallas as pl
from jax.experimental.pallas import tpu as pltpu
from jax.sharding import PartitionSpec as P

neg_large = -1e30

resp_parts = (("y_lo", 4), ("z", 8), ("core", 2))
mp_parts = (("y_hi", 2), ("x", 4))
resp_axes = tuple(name for name, _ in resp_parts)
mp_axes = tuple(name for name, _ in mp_parts)
axis_size = dict(resp_parts + mp_parts)


def gather_by_all_to_all(x, axes):
    count = int(np.prod([axis_size[a] for a in axes]))
    copies = jnp.broadcast_to(x[None], (count,) + x.shape)
    got = lax.all_to_all(copies, axes, 0, 0, tiled=True)
    return got.reshape((count * x.shape[0],) + x.shape[1:])


def attend_kernel(length_ref, q_ref, far_keys_ref, far_values_ref, near_keys_ref, near_values_ref, weight_ref, out_ref, part_ref, *, factor):
    length = length_ref[0]
    q = q_ref[...]
    far = jnp.dot(q, far_keys_ref[...], preferred_element_type=jnp.float32) * factor
    near = jnp.dot(q, near_keys_ref[...], preferred_element_type=jnp.float32) * factor
    query_pos = lax.broadcasted_iota(jnp.int32, near.shape, 0)
    key_pos = lax.broadcasted_iota(jnp.int32, near.shape, 1)
    allowed = (key_pos <= query_pos) & (key_pos < length)
    near = jnp.where(allowed, near, neg_large)
    top = jnp.maximum(jnp.max(far, axis=1, keepdims=True), jnp.max(near, axis=1, keepdims=True))
    far_w = jnp.exp(far - top)
    near_w = jnp.where(allowed, jnp.exp(near - top), 0.0)
    total = jnp.sum(far_w, axis=1, keepdims=True) + jnp.sum(near_w, axis=1, keepdims=True)
    mixed = jnp.dot(far_w.astype(jnp.bfloat16), far_values_ref[...], preferred_element_type=jnp.float32)
    mixed = mixed + jnp.dot(near_w.astype(jnp.bfloat16), near_values_ref[...], preferred_element_type=jnp.float32)
    mixed = mixed / total
    live = lax.broadcasted_iota(jnp.int32, mixed.shape, 0) < length
    rounded = jnp.where(live, mixed, 0.0).astype(out_ref.dtype)
    out_ref[...] = rounded
    weighted = rounded.astype(jnp.float32) * weight_ref[...]
    rows, lanes = weighted.shape
    part_ref[...] = jnp.sum(weighted.reshape(rows // 8, 8, lanes), axis=0)[None]


def attend(lengths, queries, far_keys_t, far_values, near_keys_t, near_values, score_weight):
    tokens, heads, head_size = queries.shape
    flat = queries.reshape(tokens, heads * head_size)
    keys = far_values.shape[0]
    kernel = functools.partial(attend_kernel, factor=1.0 / math.sqrt(head_size))
    whole = lambda h: (0, 0)
    return pl.pallas_call(
        kernel,
        grid=(heads,),
        in_specs=[
            pl.BlockSpec(memory_space=pltpu.SMEM),
            pl.BlockSpec((tokens, head_size), lambda h: (0, h)),
            pl.BlockSpec((head_size, keys), whole),
            pl.BlockSpec((keys, head_size), whole),
            pl.BlockSpec((head_size, tokens), whole),
            pl.BlockSpec((tokens, head_size), whole),
            pl.BlockSpec((1, head_size), lambda h: (0, h)),
        ],
        out_specs=[
            pl.BlockSpec((tokens, head_size), lambda h: (0, h)),
            pl.BlockSpec((1, 8, head_size), lambda h: (h, 0, 0)),
        ],
        out_shape=[
            jax.ShapeDtypeStruct((tokens, heads * head_size), jnp.bfloat16),
            jax.ShapeDtypeStruct((heads, 8, head_size), jnp.float32),
        ],
    )(lengths, flat, far_keys_t, far_values, near_keys_t, near_values, score_weight.reshape(1, -1))


def per_device(queries, response_kv, prefix_kv, lengths, score_weight):
    resp_len, local_heads, head_size = queries.shape
    length = lengths[0]
    spread_axes = ("y_lo", "z") + mp_axes
    groups = int(np.prod([axis_size[a] for a in ("y_lo", "z")]))
    by_head = jnp.transpose(prefix_kv, (2, 0, 1, 3))
    pieces = jnp.broadcast_to(by_head[None], (groups,) + by_head.shape)
    pieces = pieces.reshape((groups * by_head.shape[0],) + by_head.shape[1:])
    half = lax.all_to_all(pieces, spread_axes, 0, 0, tiled=True)
    half = half.reshape((-1,) + half.shape[2:])
    collected = gather_by_all_to_all(half, ("core",))
    far_keys_t = collected[:, 0].T
    far_values = collected[:, 1]
    near_keys_t = response_kv[:, 0, 0].T
    near_values = response_kv[:, 1, 0]
    attended, parts = attend(lengths, queries, far_keys_t, far_values, near_keys_t, near_values, score_weight)
    partial_score = jnp.sum(parts)
    spread = jnp.broadcast_to(partial_score, (axis_size["y_hi"] * axis_size["x"],))
    summed = jnp.sum(lax.all_to_all(spread, mp_axes, 0, 0, tiled=True))
    score = (summed / length.astype(jnp.float32)).reshape(1)
    return (attended, score)


def solution(mesh):
    sizes = tuple(n for _, n in resp_parts) + tuple(n for _, n in mp_parts)
    fine = jax.sharding.Mesh(np.asarray(mesh.devices).reshape(sizes), resp_axes + mp_axes)
    R, M = resp_axes, mp_axes
    in_specs = (
        P(R, M, None),
        P(R, None, M, None),
        P(R + M, None, None, None),
        P(R),
        P(M),
    )
    out_specs = (P(R, M), P(R))
    return jax.shard_map(
        per_device, mesh=fine, in_specs=in_specs, out_specs=out_specs, check_vma=False
    )
```

```python
import functools
import math

import jax
import jax.numpy as jnp
import numpy as np
from jax import lax
from jax.experimental import pallas as pl
from jax.experimental.pallas import tpu as pltpu
from jax.sharding import PartitionSpec as P

neg_large = -1e30

resp_parts = (("y_lo", 4), ("z", 8), ("core", 2))
mp_parts = (("y_hi", 2), ("x", 4))
resp_axes = tuple(name for name, _ in resp_parts)
mp_axes = tuple(name for name, _ in mp_parts)
axis_size = dict(resp_parts + mp_parts)


def gather_by_all_to_all(x, axes):
    count = int(np.prod([axis_size[a] for a in axes]))
    copies = jnp.broadcast_to(x[None], (count,) + x.shape)
    got = lax.all_to_all(copies, axes, 0, 0, tiled=True)
    return got.reshape((count * x.shape[0],) + x.shape[1:])


def attend_kernel(length_ref, q_ref, far_keys_ref, far_values_ref, near_keys_ref, near_values_ref, weight_ref, out_ref, part_ref, *, factor, chunk):
    head, block = pl.program_id(0), pl.program_id(1)
    length = length_ref[0]
    rows, head_size = q_ref.shape
    steps = far_values_ref.shape[0] // chunk
    q = q_ref[...]
    near = jnp.dot(q, near_keys_ref[...], preferred_element_type=jnp.float32)
    query_pos = lax.broadcasted_iota(jnp.int32, near.shape, 0) + block * rows
    key_pos = lax.broadcasted_iota(jnp.int32, near.shape, 1)
    allowed = (key_pos <= query_pos) & (key_pos < length)

    def far_scores(c):
        start = pl.multiple_of(c * chunk, chunk)
        return jnp.dot(q, far_keys_ref[:, pl.ds(start, chunk)], preferred_element_type=jnp.float32), start

    def widest(c, best):
        scores, _ = far_scores(c)
        return jnp.maximum(best, scores)

    best = lax.fori_loop(0, steps, widest, jnp.full((rows, chunk), neg_large, jnp.float32))
    top = jnp.maximum(jnp.max(best, axis=1, keepdims=True), jnp.max(jnp.where(allowed, near, neg_large), axis=1, keepdims=True)) * factor

    def absorb(c, carry):
        sums, accum = carry
        scores, start = far_scores(c)
        weights = jnp.exp(scores * factor - top)
        accum = accum + jnp.dot(weights.astype(jnp.bfloat16), far_values_ref[pl.ds(start, chunk), :], preferred_element_type=jnp.float32)
        return sums + weights, accum

    zeros = jnp.zeros((rows, chunk), jnp.float32)
    sums, accum = lax.fori_loop(0, steps, absorb, (zeros, jnp.zeros((rows, head_size), jnp.float32)))
    near_w = jnp.where(allowed, jnp.exp(near * factor - top), 0.0)
    total = jnp.sum(sums, axis=1, keepdims=True) + jnp.sum(near_w, axis=1, keepdims=True)
    accum = accum + jnp.dot(near_w.astype(jnp.bfloat16), near_values_ref[...], preferred_element_type=jnp.float32)
    mixed = accum / total
    live = lax.broadcasted_iota(jnp.int32, mixed.shape, 0) + block * rows < length
    rounded = jnp.where(live, mixed, 0.0).astype(out_ref.dtype)
    out_ref[...] = rounded
    weighted = rounded.astype(jnp.float32) * weight_ref[...]
    folded = jnp.sum(weighted.reshape(rows // 8, 8, head_size), axis=0)

    @pl.when((head == 0) & (block == 0))
    def _():
        part_ref[...] = jnp.zeros_like(part_ref)

    part_ref[...] += folded

    @pl.when((head == pl.num_programs(0) - 1) & (block == pl.num_programs(1) - 1))
    def _():
        part_ref[...] = jnp.broadcast_to(jnp.sum(part_ref[...]), part_ref.shape)


def attend(lengths, queries, far_keys_t, far_values, near_keys_t, near_values, score_weight, copies):
    tokens, heads, head_size = queries.shape
    flat = queries.reshape(tokens, heads * head_size)
    keys = far_values.shape[0]
    rows = 128
    kernel = functools.partial(attend_kernel, factor=1.0 / math.sqrt(head_size), chunk=128)
    whole = lambda h, b: (0, 0)
    return pl.pallas_call(
        kernel,
        grid=(heads, tokens // rows),
        in_specs=[
            pl.BlockSpec(memory_space=pltpu.SMEM),
            pl.BlockSpec((rows, head_size), lambda h, b: (b, h)),
            pl.BlockSpec((head_size, keys), whole),
            pl.BlockSpec((keys, head_size), whole),
            pl.BlockSpec((head_size, tokens), whole),
            pl.BlockSpec((tokens, head_size), whole),
            pl.BlockSpec((1, head_size), lambda h, b: (0, h)),
        ],
        out_specs=[
            pl.BlockSpec((rows, head_size), lambda h, b: (b, h)),
            pl.BlockSpec((copies, head_size), whole),
        ],
        out_shape=[
            jax.ShapeDtypeStruct((tokens, heads * head_size), jnp.bfloat16),
            jax.ShapeDtypeStruct((copies, head_size), jnp.float32),
        ],
    )(lengths, flat, far_keys_t, far_values, near_keys_t, near_values, score_weight.reshape(1, -1))


def per_device(queries, response_kv, prefix_kv, lengths, score_weight):
    resp_len, local_heads, head_size = queries.shape
    length = lengths[0]
    spread_axes = ("y_lo", "z") + mp_axes
    groups = int(np.prod([axis_size[a] for a in ("y_lo", "z")]))
    by_head = jnp.transpose(prefix_kv, (2, 0, 1, 3))
    pieces = jnp.broadcast_to(by_head[None], (groups,) + by_head.shape)
    pieces = pieces.reshape((groups * by_head.shape[0],) + by_head.shape[1:])
    half = lax.all_to_all(pieces, spread_axes, 0, 0, tiled=True)
    half = half.reshape((-1,) + half.shape[2:])
    collected = gather_by_all_to_all(half, ("core",))
    far_keys_t = collected[:, 0].T
    far_values = collected[:, 1]
    near_keys_t = response_kv[:, 0, 0].T
    near_values = response_kv[:, 1, 0]
    copies = axis_size["y_hi"] * axis_size["x"]
    attended, spread = attend(lengths, queries, far_keys_t, far_values, near_keys_t, near_values, score_weight, copies)
    summed = jnp.sum(lax.all_to_all(spread, mp_axes, 0, 0, tiled=True)[:, 0])
    score = (summed / length.astype(jnp.float32)).reshape(1)
    return (attended, score)


def solution(mesh):
    sizes = tuple(n for _, n in resp_parts) + tuple(n for _, n in mp_parts)
    fine = jax.sharding.Mesh(np.asarray(mesh.devices).reshape(sizes), resp_axes + mp_axes)
    R, M = resp_axes, mp_axes
    in_specs = (
        P(R, M, None),
        P(R, None, M, None),
        P(R + M, None, None, None),
        P(R),
        P(M),
    )
    out_specs = (P(R, M), P(R))
    return jax.shard_map(
        per_device, mesh=fine, in_specs=in_specs, out_specs=out_specs, check_vma=False
    )
```

```python
import functools
import math

import jax
import jax.numpy as jnp
import numpy as np
from jax import lax
from jax.experimental import pallas as pl
from jax.experimental.pallas import tpu as pltpu
from jax.sharding import PartitionSpec as P

neg_large = -1e30

resp_parts = (("y_lo", 4), ("z", 8), ("core", 2))
mp_parts = (("y_hi", 2), ("x", 4))
resp_axes = tuple(name for name, _ in resp_parts)
mp_axes = tuple(name for name, _ in mp_parts)
axis_size = dict(resp_parts + mp_parts)


def gather_by_all_to_all(x, axes):
    count = int(np.prod([axis_size[a] for a in axes]))
    copies = jnp.broadcast_to(x[None], (count,) + x.shape)
    got = lax.all_to_all(copies, axes, 0, 0, tiled=True)
    return got.reshape((count * x.shape[0],) + x.shape[1:])


def attend_kernel(length_ref, q_ref, far_keys_ref, far_values_ref, near_keys_ref, near_values_ref, weight_ref, out_ref, part_ref, *, factor):
    head = pl.program_id(0)
    length = length_ref[0]
    q = q_ref[...]
    far = jnp.dot(q, far_keys_ref[...], preferred_element_type=jnp.float32) * factor
    near = jnp.dot(q, near_keys_ref[...], preferred_element_type=jnp.float32) * factor
    query_pos = lax.broadcasted_iota(jnp.int32, near.shape, 0)
    key_pos = lax.broadcasted_iota(jnp.int32, near.shape, 1)
    allowed = (key_pos <= query_pos) & (key_pos < length)
    near = jnp.where(allowed, near, neg_large)
    top = jnp.maximum(jnp.max(far, axis=1, keepdims=True), jnp.max(near, axis=1, keepdims=True))
    far_w = jnp.exp(far - top)
    near_w = jnp.where(allowed, jnp.exp(near - top), 0.0)
    total = jnp.sum(far_w, axis=1, keepdims=True) + jnp.sum(near_w, axis=1, keepdims=True)
    mixed = jnp.dot(far_w.astype(jnp.bfloat16), far_values_ref[...], preferred_element_type=jnp.float32)
    mixed = mixed + jnp.dot(near_w.astype(jnp.bfloat16), near_values_ref[...], preferred_element_type=jnp.float32)
    mixed = mixed / total
    live = lax.broadcasted_iota(jnp.int32, mixed.shape, 0) < length
    rounded = jnp.where(live, mixed, 0.0).astype(out_ref.dtype)
    out_ref[...] = rounded
    weighted = rounded.astype(jnp.float32) * weight_ref[...]
    rows, lanes = weighted.shape
    folded = jnp.sum(weighted.reshape(rows // 8, 8, lanes), axis=0)

    @pl.when(head == 0)
    def _():
        part_ref[...] = jnp.zeros_like(part_ref)

    part_ref[...] += folded

    @pl.when(head == pl.num_programs(0) - 1)
    def _():
        part_ref[...] = jnp.broadcast_to(jnp.sum(part_ref[...]), part_ref.shape)


def attend(lengths, queries, far_keys_t, far_values, near_keys_t, near_values, score_weight, copies):
    tokens, heads, head_size = queries.shape
    flat = queries.reshape(tokens, heads * head_size)
    keys = far_values.shape[0]
    kernel = functools.partial(attend_kernel, factor=1.0 / math.sqrt(head_size))
    whole = lambda h: (0, 0)
    return pl.pallas_call(
        kernel,
        grid=(heads,),
        in_specs=[
            pl.BlockSpec(memory_space=pltpu.SMEM),
            pl.BlockSpec((tokens, head_size), lambda h: (0, h)),
            pl.BlockSpec((head_size, keys), whole),
            pl.BlockSpec((keys, head_size), whole),
            pl.BlockSpec((head_size, tokens), whole),
            pl.BlockSpec((tokens, head_size), whole),
            pl.BlockSpec((1, head_size), lambda h: (0, h)),
        ],
        out_specs=[
            pl.BlockSpec((tokens, head_size), lambda h: (0, h)),
            pl.BlockSpec((copies, head_size), whole),
        ],
        out_shape=[
            jax.ShapeDtypeStruct((tokens, heads * head_size), jnp.bfloat16),
            jax.ShapeDtypeStruct((copies, head_size), jnp.float32),
        ],
    )(lengths, flat, far_keys_t, far_values, near_keys_t, near_values, score_weight.reshape(1, -1))


def per_device(queries, response_kv, prefix_kv, lengths, score_weight):
    resp_len, local_heads, head_size = queries.shape
    length = lengths[0]
    spread_axes = ("y_lo", "z") + mp_axes
    groups = int(np.prod([axis_size[a] for a in ("y_lo", "z")]))
    by_head = jnp.transpose(prefix_kv, (2, 0, 1, 3))
    pieces = jnp.broadcast_to(by_head[None], (groups,) + by_head.shape)
    pieces = pieces.reshape((groups * by_head.shape[0],) + by_head.shape[1:])
    half = lax.all_to_all(pieces, spread_axes, 0, 0, tiled=True)
    half = half.reshape((-1,) + half.shape[2:])
    collected = gather_by_all_to_all(half, ("core",))
    far_keys_t = collected[:, 0].T
    far_values = collected[:, 1]
    near_keys_t = response_kv[:, 0, 0].T
    near_values = response_kv[:, 1, 0]
    copies = axis_size["y_hi"] * axis_size["x"]
    attended, spread = attend(lengths, queries, far_keys_t, far_values, near_keys_t, near_values, score_weight, copies)
    summed = jnp.sum(lax.all_to_all(spread, mp_axes, 0, 0, tiled=True)[:, 0])
    score = (summed / length.astype(jnp.float32)).reshape(1)
    return (attended, score)


def solution(mesh):
    sizes = tuple(n for _, n in resp_parts) + tuple(n for _, n in mp_parts)
    fine = jax.sharding.Mesh(np.asarray(mesh.devices).reshape(sizes), resp_axes + mp_axes)
    R, M = resp_axes, mp_axes
    in_specs = (
        P(R, M, None),
        P(R, None, M, None),
        P(R + M, None, None, None),
        P(R),
        P(M),
    )
    out_specs = (P(R, M), P(R))
    return jax.shard_map(
        per_device, mesh=fine, in_specs=in_specs, out_specs=out_specs, check_vma=False
    )
```

```python
import functools
import math

import jax
import jax.numpy as jnp
import numpy as np
from jax import lax
from jax.experimental import pallas as pl
from jax.experimental.pallas import tpu as pltpu
from jax.sharding import PartitionSpec as P


neg_large = -1e30

resp_parts = (("y_lo", 4), ("z", 8), ("core", 2))
mp_parts = (("y_hi", 2), ("x", 4))
resp_axes = tuple(name for name, _ in resp_parts)
mp_axes = tuple(name for name, _ in mp_parts)
axis_size = dict(resp_parts + mp_parts)


def gather_by_all_to_all(x, axes):
    count = int(np.prod([axis_size[a] for a in axes]))
    copies = jnp.broadcast_to(x[None], (count,) + x.shape)
    got = lax.all_to_all(copies, axes, 0, 0, tiled=True)
    return got.reshape((count * x.shape[0],) + x.shape[1:])


def first_kernel(length_ref, q_ref, far_keys_ref, far_values_ref, near_keys_ref, near_values_ref, top_ref, total_ref, accum_ref, *, factor):
    length = length_ref[0]
    q = q_ref[...]
    far = jnp.dot(q, far_keys_ref[...], preferred_element_type=jnp.float32) * factor
    near = jnp.dot(q, near_keys_ref[...], preferred_element_type=jnp.float32) * factor
    query_pos = lax.broadcasted_iota(jnp.int32, near.shape, 0)
    key_pos = lax.broadcasted_iota(jnp.int32, near.shape, 1)
    allowed = (key_pos <= query_pos) & (key_pos < length)
    near = jnp.where(allowed, near, neg_large)
    top = jnp.maximum(jnp.max(far, axis=1, keepdims=True), jnp.max(near, axis=1, keepdims=True))
    far_w = jnp.exp(far - top)
    near_w = jnp.where(allowed, jnp.exp(near - top), 0.0)
    total = jnp.sum(far_w, axis=1, keepdims=True) + jnp.sum(near_w, axis=1, keepdims=True)
    mixed = jnp.dot(far_w.astype(jnp.bfloat16), far_values_ref[...], preferred_element_type=jnp.float32)
    mixed = mixed + jnp.dot(near_w.astype(jnp.bfloat16), near_values_ref[...], preferred_element_type=jnp.float32)
    top_ref[...] = jnp.broadcast_to(top, top_ref.shape)
    total_ref[...] = jnp.broadcast_to(total, total_ref.shape)
    accum_ref[...] = mixed


def second_kernel(length_ref, q_ref, far_keys_ref, far_values_ref, top_ref, total_ref, accum_ref, weight_ref, out_ref, part_ref, *, factor):
    head = pl.program_id(0)
    length = length_ref[0]
    q = q_ref[...]
    far = jnp.dot(q, far_keys_ref[...], preferred_element_type=jnp.float32) * factor
    before = top_ref[:, :1]
    top = jnp.maximum(before, jnp.max(far, axis=1, keepdims=True))
    shrink = jnp.exp(before - top)
    far_w = jnp.exp(far - top)
    total = total_ref[:, :1] * shrink + jnp.sum(far_w, axis=1, keepdims=True)
    mixed = accum_ref[...] * shrink + jnp.dot(far_w.astype(jnp.bfloat16), far_values_ref[...], preferred_element_type=jnp.float32)
    mixed = mixed / total
    live = lax.broadcasted_iota(jnp.int32, mixed.shape, 0) < length
    rounded = jnp.where(live, mixed, 0.0).astype(out_ref.dtype)
    out_ref[...] = rounded
    weighted = rounded.astype(jnp.float32) * weight_ref[...]
    rows, lanes = weighted.shape
    folded = jnp.sum(weighted.reshape(rows // 8, 8, lanes), axis=0)

    @pl.when(head == 0)
    def _():
        part_ref[...] = jnp.zeros_like(part_ref)

    part_ref[...] += folded

    @pl.when(head == pl.num_programs(0) - 1)
    def _():
        part_ref[...] = jnp.broadcast_to(jnp.sum(part_ref[...]), part_ref.shape)


def attend_first(lengths, flat, far_keys_t, far_values, near_keys_t, near_values, head_size):
    tokens = flat.shape[0]
    heads = flat.shape[1] // head_size
    keys = far_values.shape[0]
    kernel = functools.partial(first_kernel, factor=1.0 / math.sqrt(head_size))
    whole = lambda h: (0, 0)
    per_head = pl.BlockSpec((tokens, head_size), lambda h: (0, h))
    state = jax.ShapeDtypeStruct((tokens, heads * head_size), jnp.float32)
    return pl.pallas_call(
        kernel,
        grid=(heads,),
        in_specs=[
            pl.BlockSpec(memory_space=pltpu.SMEM),
            per_head,
            pl.BlockSpec((head_size, keys), whole),
            pl.BlockSpec((keys, head_size), whole),
            pl.BlockSpec((head_size, tokens), whole),
            pl.BlockSpec((tokens, head_size), whole),
        ],
        out_specs=[per_head, per_head, per_head],
        out_shape=[state, state, state],
    )(lengths, flat, far_keys_t, far_values, near_keys_t, near_values)


def attend_second(lengths, flat, far_keys_t, far_values, top, total, accum, score_weight, head_size, copies):
    tokens = flat.shape[0]
    heads = flat.shape[1] // head_size
    keys = far_values.shape[0]
    kernel = functools.partial(second_kernel, factor=1.0 / math.sqrt(head_size))
    whole = lambda h: (0, 0)
    per_head = pl.BlockSpec((tokens, head_size), lambda h: (0, h))
    return pl.pallas_call(
        kernel,
        grid=(heads,),
        in_specs=[
            pl.BlockSpec(memory_space=pltpu.SMEM),
            per_head,
            pl.BlockSpec((head_size, keys), whole),
            pl.BlockSpec((keys, head_size), whole),
            per_head,
            per_head,
            per_head,
            pl.BlockSpec((1, head_size), lambda h: (0, h)),
        ],
        out_specs=[per_head, pl.BlockSpec((copies, head_size), whole)],
        out_shape=[
            jax.ShapeDtypeStruct((tokens, heads * head_size), jnp.bfloat16),
            jax.ShapeDtypeStruct((copies, head_size), jnp.float32),
        ],
    )(lengths, flat, far_keys_t, far_values, top, total, accum, score_weight.reshape(1, -1))


def fetch_prompt(by_head):
    spread_axes = ("y_lo", "z") + mp_axes
    groups = int(np.prod([axis_size[a] for a in ("y_lo", "z")]))
    pieces = jnp.broadcast_to(by_head[None], (groups,) + by_head.shape)
    pieces = pieces.reshape((groups * by_head.shape[0],) + by_head.shape[1:])
    half = lax.all_to_all(pieces, spread_axes, 0, 0, tiled=True)
    half = half.reshape((-1,) + half.shape[2:])
    collected = gather_by_all_to_all(half, ("core",))
    return collected[:, 0].T, collected[:, 1]


def per_device_body(queries, response_kv, prefix_kv, lengths, score_weight):
    resp_len, local_heads, head_size = queries.shape
    length = lengths[0]
    by_head = jnp.transpose(prefix_kv, (2, 0, 1, 3))
    split = by_head.shape[1] // 2
    keys_a, values_a = fetch_prompt(by_head[:, :split])
    keys_b, values_b = fetch_prompt(by_head[:, split:])
    flat = queries.reshape(resp_len, local_heads * head_size)
    near_keys_t = response_kv[:, 0, 0].T
    near_values = response_kv[:, 1, 0]
    top, total, accum = attend_first(lengths, flat, keys_a, values_a, near_keys_t, near_values, head_size)
    copies = axis_size["y_hi"] * axis_size["x"]
    attended, spread = attend_second(lengths, flat, keys_b, values_b, top, total, accum, score_weight, head_size, copies)
    summed = jnp.sum(lax.all_to_all(spread, mp_axes, 0, 0, tiled=True)[:, 0])
    score = (summed / length.astype(jnp.float32)).reshape(1)
    return (attended, score)


def solution(mesh):
    sizes = tuple(n for _, n in resp_parts) + tuple(n for _, n in mp_parts)
    fine = jax.sharding.Mesh(np.asarray(mesh.devices).reshape(sizes), resp_axes + mp_axes)
    R, M = resp_axes, mp_axes
    in_specs = (
        P(R, M, None),
        P(R, None, M, None),
        P(R + M, None, None, None),
        P(R),
        P(M),
    )
    out_specs = (P(R, M), P(R))
    return jax.shard_map(per_device_body, mesh=fine, in_specs=in_specs, out_specs=out_specs, check_vma=False)
```

```python
import functools
import math

import jax
import jax.numpy as jnp
import numpy as np
from jax import lax
from jax.experimental import pallas as pl
from jax.experimental.pallas import tpu as pltpu
from jax.sharding import PartitionSpec as P

neg_large = -1e30

resp_parts = (("y_lo", 4), ("z", 8), ("core", 2))
mp_parts = (("y_hi", 2), ("x", 4))
resp_axes = tuple(name for name, _ in resp_parts)
mp_axes = tuple(name for name, _ in mp_parts)
axis_size = dict(resp_parts + mp_parts)


def gather_by_all_to_all(x, axes):
    count = int(np.prod([axis_size[a] for a in axes]))
    copies = jnp.broadcast_to(x[None], (count,) + x.shape)
    got = lax.all_to_all(copies, axes, 0, 0, tiled=True)
    return got.reshape((count * x.shape[0],) + x.shape[1:])


def attend_kernel(length_ref, q_ref, far_ref, near_keys_ref, near_values_ref, weight_ref, out_ref, part_ref, *, factor):
    head = pl.program_id(0)
    length = length_ref[0]
    q = q_ref[...]
    head_size = q.shape[1]
    contract = (((1,), (1,)), ((), ()))
    far = lax.dot_general(q, far_ref[:, :head_size], contract, preferred_element_type=jnp.float32) * factor
    near = jnp.dot(q, near_keys_ref[...], preferred_element_type=jnp.float32) * factor
    query_pos = lax.broadcasted_iota(jnp.int32, near.shape, 0)
    key_pos = lax.broadcasted_iota(jnp.int32, near.shape, 1)
    allowed = (key_pos <= query_pos) & (key_pos < length)
    near = jnp.where(allowed, near, neg_large)
    top = jnp.maximum(jnp.max(far, axis=1, keepdims=True), jnp.max(near, axis=1, keepdims=True))
    far_w = jnp.exp(far - top)
    near_w = jnp.where(allowed, jnp.exp(near - top), 0.0)
    total = jnp.sum(far_w, axis=1, keepdims=True) + jnp.sum(near_w, axis=1, keepdims=True)
    mixed = jnp.dot(far_w.astype(jnp.bfloat16), far_ref[:, head_size:], preferred_element_type=jnp.float32)
    mixed = mixed + jnp.dot(near_w.astype(jnp.bfloat16), near_values_ref[...], preferred_element_type=jnp.float32)
    mixed = mixed / total
    live = lax.broadcasted_iota(jnp.int32, mixed.shape, 0) < length
    rounded = jnp.where(live, mixed, 0.0).astype(out_ref.dtype)
    out_ref[...] = rounded
    weighted = rounded.astype(jnp.float32) * weight_ref[...]
    rows, lanes = weighted.shape
    folded = jnp.sum(weighted.reshape(rows // 8, 8, lanes), axis=0)

    @pl.when(head == 0)
    def _():
        part_ref[...] = jnp.zeros_like(part_ref)

    part_ref[...] += folded

    @pl.when(head == pl.num_programs(0) - 1)
    def _():
        part_ref[...] = jnp.broadcast_to(jnp.sum(part_ref[...]), part_ref.shape)


def attend(lengths, queries, far_kv, near_keys_t, near_values, score_weight, copies):
    tokens, heads, head_size = queries.shape
    flat = queries.reshape(tokens, heads * head_size)
    keys = far_kv.shape[0]
    kernel = functools.partial(attend_kernel, factor=1.0 / math.sqrt(head_size))
    whole = lambda h: (0, 0)
    return pl.pallas_call(
        kernel,
        grid=(heads,),
        in_specs=[
            pl.BlockSpec(memory_space=pltpu.SMEM),
            pl.BlockSpec((tokens, head_size), lambda h: (0, h)),
            pl.BlockSpec((keys, 2 * head_size), whole),
            pl.BlockSpec((head_size, tokens), whole),
            pl.BlockSpec((tokens, head_size), whole),
            pl.BlockSpec((1, head_size), lambda h: (0, h)),
        ],
        out_specs=[
            pl.BlockSpec((tokens, head_size), lambda h: (0, h)),
            pl.BlockSpec((copies, head_size), whole),
        ],
        out_shape=[
            jax.ShapeDtypeStruct((tokens, heads * head_size), jnp.bfloat16),
            jax.ShapeDtypeStruct((copies, head_size), jnp.float32),
        ],
    )(lengths, flat, far_kv, near_keys_t, near_values, score_weight.reshape(1, -1))


def per_device(queries, response_kv, prefix_kv, lengths, score_weight):
    resp_len, local_heads, head_size = queries.shape
    length = lengths[0]
    spread_axes = ("y_lo", "z") + mp_axes
    groups = int(np.prod([axis_size[a] for a in ("y_lo", "z")]))
    by_head = jnp.transpose(prefix_kv, (2, 0, 1, 3))
    pieces = jnp.broadcast_to(by_head[None], (groups,) + by_head.shape)
    pieces = pieces.reshape((groups * by_head.shape[0],) + by_head.shape[1:])
    half = lax.all_to_all(pieces, spread_axes, 0, 0, tiled=True)
    half = half.reshape((-1,) + half.shape[2:])
    collected = gather_by_all_to_all(half, ("core",))
    far_kv = collected.reshape(collected.shape[0], 2 * head_size)
    near_keys_t = response_kv[:, 0, 0].T
    near_values = response_kv[:, 1, 0]
    copies = axis_size["y_hi"] * axis_size["x"]
    attended, spread = attend(lengths, queries, far_kv, near_keys_t, near_values, score_weight, copies)
    summed = jnp.sum(lax.all_to_all(spread, mp_axes, 0, 0, tiled=True)[:, 0])
    score = (summed / length.astype(jnp.float32)).reshape(1)
    return (attended, score)


def solution(mesh):
    sizes = tuple(n for _, n in resp_parts) + tuple(n for _, n in mp_parts)
    fine = jax.sharding.Mesh(np.asarray(mesh.devices).reshape(sizes), resp_axes + mp_axes)
    R, M = resp_axes, mp_axes
    in_specs = (
        P(R, M, None),
        P(R, None, M, None),
        P(R + M, None, None, None),
        P(R),
        P(M),
    )
    out_specs = (P(R, M), P(R))
    return jax.shard_map(
        per_device, mesh=fine, in_specs=in_specs, out_specs=out_specs, check_vma=False
    )
```

```python
import functools
import math

import jax
import jax.numpy as jnp
import numpy as np
from jax import lax
from jax.experimental import pallas as pl
from jax.experimental.pallas import tpu as pltpu
from jax.sharding import PartitionSpec as P

neg_large = -1e30

resp_parts = (("y_lo", 4), ("z", 8), ("core", 2))
mp_parts = (("y_hi", 2), ("x", 4))
resp_axes = tuple(name for name, _ in resp_parts)
mp_axes = tuple(name for name, _ in mp_parts)
axis_size = dict(resp_parts + mp_parts)


def gather_by_all_to_all(x, axes):
    count = int(np.prod([axis_size[a] for a in axes]))
    copies = jnp.broadcast_to(x[None], (count,) + x.shape)
    got = lax.all_to_all(copies, axes, 0, 0, tiled=True)
    return got.reshape((count * x.shape[0],) + x.shape[1:])


def attend_kernel(length_ref, q_ref, far_keys_ref, far_values_ref, near_keys_ref, near_values_ref, weight_ref, out_ref, part_ref, *, factor):
    head = pl.program_id(0)
    length = length_ref[0]
    q = q_ref[...]
    far = jnp.dot(q, far_keys_ref[...], preferred_element_type=jnp.float32) * factor
    near = jnp.dot(q, near_keys_ref[...], preferred_element_type=jnp.float32) * factor
    query_pos = lax.broadcasted_iota(jnp.int32, near.shape, 0)
    key_pos = lax.broadcasted_iota(jnp.int32, near.shape, 1)
    allowed = (key_pos <= query_pos) & (key_pos < length)
    near = jnp.where(allowed, near, neg_large)
    top = jnp.maximum(jnp.max(far, axis=1, keepdims=True), jnp.max(near, axis=1, keepdims=True))
    far_w = jnp.exp(far - top)
    near_w = jnp.where(allowed, jnp.exp(near - top), 0.0)
    total = jnp.sum(far_w, axis=1, keepdims=True) + jnp.sum(near_w, axis=1, keepdims=True)
    mixed = jnp.dot(far_w.astype(jnp.bfloat16), far_values_ref[...], preferred_element_type=jnp.float32)
    mixed = mixed + jnp.dot(near_w.astype(jnp.bfloat16), near_values_ref[...], preferred_element_type=jnp.float32)
    mixed = mixed / total
    live = lax.broadcasted_iota(jnp.int32, mixed.shape, 0) < length
    rounded = jnp.where(live, mixed, 0.0).astype(out_ref.dtype)
    out_ref[...] = rounded
    weighted = rounded.astype(jnp.float32) * weight_ref[...]
    rows, lanes = weighted.shape
    folded = jnp.sum(weighted.reshape(rows // 8, 8, lanes), axis=0)

    @pl.when(head == 0)
    def _():
        part_ref[...] = jnp.zeros_like(part_ref)

    part_ref[...] += folded

    @pl.when(head == pl.num_programs(0) - 1)
    def _():
        part_ref[...] = jnp.broadcast_to(jnp.sum(part_ref[...]), part_ref.shape)


def attend(lengths, queries, far_keys_t, far_values, near_keys_t, near_values, score_weight, copies):
    tokens, heads, head_size = queries.shape
    flat = queries.reshape(tokens, heads * head_size)
    keys = far_values.shape[0]
    kernel = functools.partial(attend_kernel, factor=1.0 / math.sqrt(head_size))
    whole = lambda h: (0, 0)
    return pl.pallas_call(
        kernel,
        grid=(heads,),
        in_specs=[
            pl.BlockSpec(memory_space=pltpu.SMEM),
            pl.BlockSpec((tokens, head_size), lambda h: (0, h)),
            pl.BlockSpec((head_size, keys), whole),
            pl.BlockSpec((keys, head_size), whole),
            pl.BlockSpec((head_size, tokens), whole),
            pl.BlockSpec((tokens, head_size), whole),
            pl.BlockSpec((1, head_size), lambda h: (0, h)),
        ],
        out_specs=[
            pl.BlockSpec((tokens, head_size), lambda h: (0, h)),
            pl.BlockSpec((copies, head_size), whole),
        ],
        out_shape=[
            jax.ShapeDtypeStruct((tokens, heads * head_size), jnp.bfloat16),
            jax.ShapeDtypeStruct((copies, head_size), jnp.float32),
        ],
    )(lengths, flat, far_keys_t, far_values, near_keys_t, near_values, score_weight.reshape(1, -1))


def per_device(queries, response_kv, prefix_kv, lengths, score_weight):
    resp_len, local_heads, head_size = queries.shape
    length = lengths[0]
    spread_axes = mp_axes + ("y_lo", "z")
    groups = int(np.prod([axis_size[a] for a in ("y_lo", "z")]))
    by_head = jnp.transpose(prefix_kv, (2, 0, 1, 3))
    pieces = jnp.broadcast_to(by_head[:, None], by_head.shape[:1] + (groups,) + by_head.shape[1:])
    pieces = pieces.reshape((groups * by_head.shape[0],) + by_head.shape[1:])
    half = lax.all_to_all(pieces, spread_axes, 0, 0, tiled=True)
    half = half.reshape((-1,) + half.shape[2:])
    collected = gather_by_all_to_all(half, ("core",))
    far_keys_t = collected[:, 0].T
    far_values = collected[:, 1]
    near_keys_t = response_kv[:, 0, 0].T
    near_values = response_kv[:, 1, 0]
    copies = axis_size["y_hi"] * axis_size["x"]
    attended, spread = attend(lengths, queries, far_keys_t, far_values, near_keys_t, near_values, score_weight, copies)
    summed = jnp.sum(lax.all_to_all(spread, mp_axes, 0, 0, tiled=True)[:, 0])
    score = (summed / length.astype(jnp.float32)).reshape(1)
    return (attended, score)


def solution(mesh):
    sizes = tuple(n for _, n in resp_parts) + tuple(n for _, n in mp_parts)
    fine = jax.sharding.Mesh(np.asarray(mesh.devices).reshape(sizes), resp_axes + mp_axes)
    R, M = resp_axes, mp_axes
    in_specs = (
        P(R, M, None),
        P(R, None, M, None),
        P(R + M, None, None, None),
        P(R),
        P(M),
    )
    out_specs = (P(R, M), P(R))
    return jax.shard_map(
        per_device, mesh=fine, in_specs=in_specs, out_specs=out_specs, check_vma=False
    )
```

```python
import functools
import math

import jax
import jax.numpy as jnp
import numpy as np
from jax import lax
from jax.experimental import pallas as pl
from jax.experimental.pallas import tpu as pltpu
from jax.sharding import PartitionSpec as P


neg_large = -1e30

resp_parts = (("y_lo", 4), ("z", 8), ("core", 2))
mp_parts = (("y_hi", 2), ("x", 4))
resp_axes = tuple(name for name, _ in resp_parts)
mp_axes = tuple(name for name, _ in mp_parts)
axis_size = dict(resp_parts + mp_parts)


def gather_by_all_to_all(x, axes):
    count = int(np.prod([axis_size[a] for a in axes]))
    copies = jnp.broadcast_to(x[None], (count,) + x.shape)
    got = lax.all_to_all(copies, axes, 0, 0, tiled=True)
    return got.reshape((count * x.shape[0],) + x.shape[1:])


def first_kernel(length_ref, q_ref, near_keys_ref, near_values_ref, top_ref, total_ref, accum_ref, *, factor):
    length = length_ref[0]
    q = q_ref[...]
    near = jnp.dot(q, near_keys_ref[...], preferred_element_type=jnp.float32) * factor
    query_pos = lax.broadcasted_iota(jnp.int32, near.shape, 0)
    key_pos = lax.broadcasted_iota(jnp.int32, near.shape, 1)
    allowed = (key_pos <= query_pos) & (key_pos < length)
    near = jnp.where(allowed, near, neg_large)
    top = jnp.max(near, axis=1, keepdims=True)
    near_w = jnp.where(allowed, jnp.exp(near - top), 0.0)
    total = jnp.sum(near_w, axis=1, keepdims=True)
    mixed = jnp.dot(near_w.astype(jnp.bfloat16), near_values_ref[...], preferred_element_type=jnp.float32)
    top_ref[...] = jnp.broadcast_to(top, top_ref.shape)
    total_ref[...] = jnp.broadcast_to(total, total_ref.shape)
    accum_ref[...] = mixed


def second_kernel(length_ref, q_ref, far_keys_ref, far_values_ref, top_ref, total_ref, accum_ref, weight_ref, out_ref, part_ref, *, factor):
    head = pl.program_id(0)
    length = length_ref[0]
    q = q_ref[...]
    far = jnp.dot(q, far_keys_ref[...], preferred_element_type=jnp.float32) * factor
    before = top_ref[:, :1]
    top = jnp.maximum(before, jnp.max(far, axis=1, keepdims=True))
    shrink = jnp.exp(before - top)
    far_w = jnp.exp(far - top)
    total = total_ref[:, :1] * shrink + jnp.sum(far_w, axis=1, keepdims=True)
    mixed = accum_ref[...] * shrink + jnp.dot(far_w.astype(jnp.bfloat16), far_values_ref[...], preferred_element_type=jnp.float32)
    mixed = mixed / total
    live = lax.broadcasted_iota(jnp.int32, mixed.shape, 0) < length
    rounded = jnp.where(live, mixed, 0.0).astype(out_ref.dtype)
    out_ref[...] = rounded
    weighted = rounded.astype(jnp.float32) * weight_ref[...]
    rows, lanes = weighted.shape
    folded = jnp.sum(weighted.reshape(rows // 8, 8, lanes), axis=0)

    @pl.when(head == 0)
    def _():
        part_ref[...] = jnp.zeros_like(part_ref)

    part_ref[...] += folded

    @pl.when(head == pl.num_programs(0) - 1)
    def _():
        part_ref[...] = jnp.broadcast_to(jnp.sum(part_ref[...]), part_ref.shape)


def attend_first(lengths, flat, near_keys_t, near_values, head_size):
    tokens = flat.shape[0]
    heads = flat.shape[1] // head_size
    kernel = functools.partial(first_kernel, factor=1.0 / math.sqrt(head_size))
    whole = lambda h: (0, 0)
    per_head = pl.BlockSpec((tokens, head_size), lambda h: (0, h))
    state = jax.ShapeDtypeStruct((tokens, heads * head_size), jnp.float32)
    return pl.pallas_call(
        kernel,
        grid=(heads,),
        in_specs=[
            pl.BlockSpec(memory_space=pltpu.SMEM),
            per_head,
            pl.BlockSpec((head_size, tokens), whole),
            pl.BlockSpec((tokens, head_size), whole),
        ],
        out_specs=[per_head, per_head, per_head],
        out_shape=[state, state, state],
    )(lengths, flat, near_keys_t, near_values)


def attend_second(lengths, flat, far_keys_t, far_values, top, total, accum, score_weight, head_size, copies):
    tokens = flat.shape[0]
    heads = flat.shape[1] // head_size
    keys = far_values.shape[0]
    kernel = functools.partial(second_kernel, factor=1.0 / math.sqrt(head_size))
    whole = lambda h: (0, 0)
    per_head = pl.BlockSpec((tokens, head_size), lambda h: (0, h))
    return pl.pallas_call(
        kernel,
        grid=(heads,),
        in_specs=[
            pl.BlockSpec(memory_space=pltpu.SMEM),
            per_head,
            pl.BlockSpec((head_size, keys), whole),
            pl.BlockSpec((keys, head_size), whole),
            per_head,
            per_head,
            per_head,
            pl.BlockSpec((1, head_size), lambda h: (0, h)),
        ],
        out_specs=[per_head, pl.BlockSpec((copies, head_size), whole)],
        out_shape=[
            jax.ShapeDtypeStruct((tokens, heads * head_size), jnp.bfloat16),
            jax.ShapeDtypeStruct((copies, head_size), jnp.float32),
        ],
    )(lengths, flat, far_keys_t, far_values, top, total, accum, score_weight.reshape(1, -1))


def fetch_prompt(by_head):
    spread_axes = ("y_lo", "z") + mp_axes
    groups = int(np.prod([axis_size[a] for a in ("y_lo", "z")]))
    pieces = jnp.broadcast_to(by_head[None], (groups,) + by_head.shape)
    pieces = pieces.reshape((groups * by_head.shape[0],) + by_head.shape[1:])
    half = lax.all_to_all(pieces, spread_axes, 0, 0, tiled=True)
    half = half.reshape((-1,) + half.shape[2:])
    collected = gather_by_all_to_all(half, ("core",))
    return collected[:, 0].T, collected[:, 1]


def per_device_body(queries, response_kv, prefix_kv, lengths, score_weight):
    resp_len, local_heads, head_size = queries.shape
    length = lengths[0]
    by_head = jnp.transpose(prefix_kv, (2, 0, 1, 3))
    keys, values = fetch_prompt(by_head)
    flat = queries.reshape(resp_len, local_heads * head_size)
    near_keys_t = response_kv[:, 0, 0].T
    near_values = response_kv[:, 1, 0]
    top, total, accum = attend_first(lengths, flat, near_keys_t, near_values, head_size)
    copies = axis_size["y_hi"] * axis_size["x"]
    attended, spread = attend_second(lengths, flat, keys, values, top, total, accum, score_weight, head_size, copies)
    summed = jnp.sum(lax.all_to_all(spread, mp_axes, 0, 0, tiled=True)[:, 0])
    score = (summed / length.astype(jnp.float32)).reshape(1)
    return (attended, score)


def solution(mesh):
    sizes = tuple(n for _, n in resp_parts) + tuple(n for _, n in mp_parts)
    fine = jax.sharding.Mesh(np.asarray(mesh.devices).reshape(sizes), resp_axes + mp_axes)
    R, M = resp_axes, mp_axes
    in_specs = (
        P(R, M, None),
        P(R, None, M, None),
        P(R + M, None, None, None),
        P(R),
        P(M),
    )
    out_specs = (P(R, M), P(R))
    return jax.shard_map(per_device_body, mesh=fine, in_specs=in_specs, out_specs=out_specs, check_vma=False)
```

```python
import functools
import math

import jax
import jax.numpy as jnp
import numpy as np
from jax import lax
from jax.experimental import pallas as pl
from jax.experimental.pallas import tpu as pltpu
from jax.sharding import PartitionSpec as P


neg_large = -1e30

resp_parts = (("y_lo", 4), ("z", 8), ("core", 2))
mp_parts = (("y_hi", 2), ("x", 4))
resp_axes = tuple(name for name, _ in resp_parts)
mp_axes = tuple(name for name, _ in mp_parts)
axis_size = dict(resp_parts + mp_parts)


def gather_by_all_to_all(x, axes):
    count = int(np.prod([axis_size[a] for a in axes]))
    copies = jnp.broadcast_to(x[None], (count,) + x.shape)
    got = lax.all_to_all(copies, axes, 0, 0, tiled=True)
    return got.reshape((count * x.shape[0],) + x.shape[1:])


def first_kernel(length_ref, q_ref, near_keys_ref, near_values_ref, top_ref, total_ref, accum_ref, *, factor):
    length = length_ref[0]
    q = q_ref[...]
    near = jnp.dot(q, near_keys_ref[...], preferred_element_type=jnp.float32) * factor
    query_pos = lax.broadcasted_iota(jnp.int32, near.shape, 0)
    key_pos = lax.broadcasted_iota(jnp.int32, near.shape, 1)
    allowed = (key_pos <= query_pos) & (key_pos < length)
    near = jnp.where(allowed, near, neg_large)
    top = jnp.max(near, axis=1, keepdims=True)
    near_w = jnp.where(allowed, jnp.exp(near - top), 0.0)
    total = jnp.sum(near_w, axis=1, keepdims=True)
    mixed = jnp.dot(near_w.astype(jnp.bfloat16), near_values_ref[...], preferred_element_type=jnp.float32)
    top_ref[...] = jnp.broadcast_to(top, top_ref.shape)
    total_ref[...] = jnp.broadcast_to(total, total_ref.shape)
    accum_ref[...] = mixed


def second_kernel(length_ref, q_ref, far_keys_ref, far_values_ref, top_ref, total_ref, accum_ref, weight_ref, out_ref, part_ref, *, factor):
    head = pl.program_id(0)
    length = length_ref[0]
    q = q_ref[...]
    contract = (((1,), (1,)), ((), ()))
    far = lax.dot_general(q, far_keys_ref[...], contract, preferred_element_type=jnp.float32) * factor
    before = top_ref[:, :1]
    top = jnp.maximum(before, jnp.max(far, axis=1, keepdims=True))
    shrink = jnp.exp(before - top)
    far_w = jnp.exp(far - top)
    total = total_ref[:, :1] * shrink + jnp.sum(far_w, axis=1, keepdims=True)
    mixed = accum_ref[...] * shrink + jnp.dot(far_w.astype(jnp.bfloat16), far_values_ref[...], preferred_element_type=jnp.float32)
    mixed = mixed / total
    live = lax.broadcasted_iota(jnp.int32, mixed.shape, 0) < length
    rounded = jnp.where(live, mixed, 0.0).astype(out_ref.dtype)
    out_ref[...] = rounded
    weighted = rounded.astype(jnp.float32) * weight_ref[...]
    rows, lanes = weighted.shape
    folded = jnp.sum(weighted.reshape(rows // 8, 8, lanes), axis=0)

    @pl.when(head == 0)
    def _():
        part_ref[...] = jnp.zeros_like(part_ref)

    part_ref[...] += folded

    @pl.when(head == pl.num_programs(0) - 1)
    def _():
        part_ref[...] = jnp.broadcast_to(jnp.sum(part_ref[...]), part_ref.shape)


def attend_first(lengths, flat, near_keys_t, near_values, head_size):
    tokens = flat.shape[0]
    heads = flat.shape[1] // head_size
    kernel = functools.partial(first_kernel, factor=1.0 / math.sqrt(head_size))
    whole = lambda h: (0, 0)
    per_head = pl.BlockSpec((tokens, head_size), lambda h: (0, h))
    state = jax.ShapeDtypeStruct((tokens, heads * head_size), jnp.float32)
    return pl.pallas_call(
        kernel,
        grid=(heads,),
        in_specs=[
            pl.BlockSpec(memory_space=pltpu.SMEM),
            per_head,
            pl.BlockSpec((head_size, tokens), whole),
            pl.BlockSpec((tokens, head_size), whole),
        ],
        out_specs=[per_head, per_head, per_head],
        out_shape=[state, state, state],
    )(lengths, flat, near_keys_t, near_values)


def attend_second(lengths, flat, far_keys, far_values, top, total, accum, score_weight, head_size, copies):
    tokens = flat.shape[0]
    heads = flat.shape[1] // head_size
    keys = far_values.shape[0]
    kernel = functools.partial(second_kernel, factor=1.0 / math.sqrt(head_size))
    whole = lambda h: (0, 0)
    per_head = pl.BlockSpec((tokens, head_size), lambda h: (0, h))
    return pl.pallas_call(
        kernel,
        grid=(heads,),
        in_specs=[
            pl.BlockSpec(memory_space=pltpu.SMEM),
            per_head,
            pl.BlockSpec((keys, head_size), whole),
            pl.BlockSpec((keys, head_size), whole),
            per_head,
            per_head,
            per_head,
            pl.BlockSpec((1, head_size), lambda h: (0, h)),
        ],
        out_specs=[per_head, pl.BlockSpec((copies, head_size), whole)],
        out_shape=[
            jax.ShapeDtypeStruct((tokens, heads * head_size), jnp.bfloat16),
            jax.ShapeDtypeStruct((copies, head_size), jnp.float32),
        ],
    )(lengths, flat, far_keys, far_values, top, total, accum, score_weight.reshape(1, -1))


def fetch_prompt(by_head):
    spread_axes = ("y_lo", "z") + mp_axes
    groups = int(np.prod([axis_size[a] for a in ("y_lo", "z")]))
    pieces = jnp.broadcast_to(by_head[None], (groups,) + by_head.shape)
    pieces = pieces.reshape((groups * by_head.shape[0],) + by_head.shape[1:])
    half = lax.all_to_all(pieces, spread_axes, 0, 0, tiled=True)
    both = gather_by_all_to_all(half[None], ("core",))
    keys = both[:, :, 0].reshape(-1, both.shape[-1])
    values = both[:, :, 1].reshape(-1, both.shape[-1])
    return keys, values


def per_device_body(queries, response_kv, prefix_kv, lengths, score_weight):
    resp_len, local_heads, head_size = queries.shape
    length = lengths[0]
    by_head = jnp.transpose(prefix_kv, (2, 1, 0, 3))
    keys, values = fetch_prompt(by_head)
    flat = queries.reshape(resp_len, local_heads * head_size)
    near_keys_t = response_kv[:, 0, 0].T
    near_values = response_kv[:, 1, 0]
    top, total, accum = attend_first(lengths, flat, near_keys_t, near_values, head_size)
    copies = axis_size["y_hi"] * axis_size["x"]
    attended, spread = attend_second(lengths, flat, keys, values, top, total, accum, score_weight, head_size, copies)
    summed = jnp.sum(lax.all_to_all(spread, mp_axes, 0, 0, tiled=True)[:, 0])
    score = (summed / length.astype(jnp.float32)).reshape(1)
    return (attended, score)


def solution(mesh):
    sizes = tuple(n for _, n in resp_parts) + tuple(n for _, n in mp_parts)
    fine = jax.sharding.Mesh(np.asarray(mesh.devices).reshape(sizes), resp_axes + mp_axes)
    R, M = resp_axes, mp_axes
    in_specs = (
        P(R, M, None),
        P(R, None, M, None),
        P(R + M, None, None, None),
        P(R),
        P(M),
    )
    out_specs = (P(R, M), P(R))
    return jax.shard_map(per_device_body, mesh=fine, in_specs=in_specs, out_specs=out_specs, check_vma=False)
```
